512 devices in a mesh: inst: 16 (over y_lo, x, core), blk: 32 (over z, y_hi).
Axes of the slice: x: 4, y: 4 (y_hi: 2, y_lo: 2; y = y_hi * 2 + y_lo), z: 16, core: 2. Of those that a mesh axis runs over, the one named last changes fastest.
Arguments:
- state: float32 [16, 2, 6, 8, 8, 4096], P('inst', None, None, None, None, 'blk'), may hold values from -0.5 to 3, as said below
- donor_block: int32 [16, 2, 32], P('inst', None, 'blk'), may hold values from 0 to 31, as said below
- donor_offset: int32 [16, 2, 32], P('inst', None, 'blk'), may hold values from 0 to 127, as said below
Outputs:
- hb_residual: float32 [16, 2, 6, 8, 8, 4096], P('inst', None, None, None, None, 'blk')
- new_state: float32 [16, 2, 6, 8, 8, 4096], P('inst', None, None, None, None, 'blk')
The draws below stay inside these ranges and needn't reach their ends.
Inputs may be any that keep to these rules, and one draw needn't show every extreme that they name: For each instance n and row r there is one rotation R with donor_block[n, r, b] = (b + R) mod 32 for every block b. `donor_offset`: for each instance and row the offset is the same for all blocks. `state`: density lies in [0.8, 1.25], momenta in [-0.5, 0.5], total energy in [2, 3], turbulence variable in [0.05, 0.5].
All inputs are finite; a program needn't handle non-finite values.
Results may differ from the reference program's by a relative error of at most 0.0003.
Values sent between devices are 32-bit elements; how exact they have to be, the bound alone decides.
No kernel may reach another device: no remote copies, remote signals or barrier semaphores. Data moves between devices by JAX's collectives and lax.ppermute only.
A program may use at most 64 MiB of HBM per device.

```python
import jax
import jax.numpy as jnp
from jax import lax

CI = 8
CJ = 8
CK = 128
INSTANCES = 16
NBLOCKS = 32


def draw_state(key, part):
    cell_shape = (INSTANCES, 2, 6, CI, CJ, CK * NBLOCKS)
    low_end = jnp.array([0.8, -0.5, -0.5, -0.5, 2.0, 0.05], jnp.float32).reshape(1, 1, 6, 1, 1, 1)
    high_end = jnp.array([1.25, 0.5, 0.5, 0.5, 3.0, 0.5], jnp.float32).reshape(1, 1, 6, 1, 1, 1)
    uniform_part = jax.random.uniform(key, cell_shape, jnp.float32)
    return low_end + (high_end - low_end) * uniform_part


def draw_donor_block(key, part):
    rotations = jax.random.randint(jax.random.fold_in(key, 11), (INSTANCES, 2, 1), 0, NBLOCKS)
    sectors = jnp.arange(NBLOCKS, dtype=jnp.int32).reshape(1, 1, NBLOCKS)
    return jnp.mod(sectors + rotations, NBLOCKS).astype(jnp.int32)


def draw_donor_offset(key, part):
    offsets = jax.random.randint(jax.random.fold_in(key, 13), (INSTANCES, 2, 1), 0, CK)
    offsets = offsets.at[0, 0, 0].set(CK - 1)
    offsets = offsets.at[0, 1, 0].set(0)
    return jnp.broadcast_to(offsets, (INSTANCES, 2, NBLOCKS)).astype(jnp.int32)


def setup_inputs(seed: int = 0) -> dict:
    streams_of = jax.random.split(jax.random.key(seed), 4)
    return {
        "state": draw_state(jax.random.fold_in(streams_of[3], 71), 0),
        "donor_block": draw_donor_block(jax.random.fold_in(streams_of[3], 71), 0),
        "donor_offset": draw_donor_offset(jax.random.fold_in(streams_of[3], 71), 0),
    }


gamma_ratio = 1.4
second_coef = 0.5
fourth_coef = 1.0 / 32.0
courant = 0.8
frequency = 0.5
highest = lax.Precision.HIGHEST

def spectral_weights(target, source, number):
    distance = jnp.mod(target - source, number)
    angle = jnp.pi / number * distance.astype(jnp.float32)
    parity = 1.0 - 2.0 * jnp.mod(distance, 2).astype(jnp.float32)
    nonzero = distance != 0
    sine_safe = jnp.where(nonzero, jnp.sin(angle), 1.0)
    cotangent = jnp.where(nonzero, jnp.cos(angle) / sine_safe, 0.0)
    return parity * (0.25 * frequency + 0.5 * frequency * cotangent)

def take_range(array, begin, length, along):
    return lax.slice_in_dim(array, begin, begin + length, axis=along)

def flux_divergence(extended, along):
    length = extended.shape[along] - 4
    cell_axis = along - 1
    density = extended[0]
    inverse = 1.0 / density
    normal_vel = extended[along] * inverse
    kinetic = 0.5 * (extended[1] ** 2 + extended[2] ** 2 + extended[3] ** 2) * inverse
    pressure = (gamma_ratio - 1.0) * (extended[4] - kinetic)
    sound = jnp.sqrt(gamma_ratio * pressure * inverse)
    momentum_flux = []
    for component in (1, 2, 3):
        if component == along:
            momentum_flux.append(extended[component] * normal_vel + pressure)
        else:
            momentum_flux.append(extended[component] * normal_vel)
    fluxes = jnp.stack([extended[along]] + momentum_flux + [(extended[4] + pressure) * normal_vel, extended[5] * normal_vel])
    radius = jnp.abs(normal_vel) + sound
    p_plus = take_range(pressure, 2, length + 2, cell_axis)
    p_here = take_range(pressure, 1, length + 2, cell_axis)
    p_minus = take_range(pressure, 0, length + 2, cell_axis)
    sensor = jnp.abs(p_plus - 2.0 * p_here + p_minus) / (p_plus + 2.0 * p_here + p_minus)
    spread = 0.5 * (take_range(radius, 1, length + 1, cell_axis) + take_range(radius, 2, length + 1, cell_axis))
    eps_two = second_coef * jnp.maximum(take_range(sensor, 0, length + 1, cell_axis), take_range(sensor, 1, length + 1, cell_axis))
    eps_four = jnp.maximum(0.0, fourth_coef - eps_two)
    first_diff = take_range(extended, 2, length + 1, along) - take_range(extended, 1, length + 1, along)
    third_diff = take_range(extended, 3, length + 1, along) - 3.0 * take_range(extended, 2, length + 1, along) + 3.0 * take_range(extended, 1, length + 1, along) - take_range(extended, 0, length + 1, along)
    interface = 0.5 * (take_range(fluxes, 1, length + 1, along) + take_range(fluxes, 2, length + 1, along)) - spread * (eps_two * first_diff - eps_four * third_diff)
    return take_range(interface, 1, length, along) - take_range(interface, 0, length, along)

def wall_extend(block):
    mirror_sign = jnp.array([1.0, 1.0, -1.0, 1.0, 1.0, 1.0], jnp.float32).reshape(6, 1, 1, 1)
    lower_ghost = block[:, :, 0:2][:, :, ::-1] * mirror_sign
    upper_ghost = block[:, :, -2:][:, :, ::-1] * mirror_sign
    return jnp.concatenate([lower_ghost, block, upper_ghost], axis=2)

def row_residual(block, low_ghost, high_ghost, circum_ext):
    axial_ext = jnp.concatenate([low_ghost, block, high_ghost], axis=1)
    return flux_divergence(axial_ext, 1) + flux_divergence(wall_extend(block), 2) + flux_divergence(circum_ext, 3)

def local_step(fields, number):
    inverse = 1.0 / fields[:, 0]
    kinetic = 0.5 * (fields[:, 1] ** 2 + fields[:, 2] ** 2 + fields[:, 3] ** 2) * inverse
    pressure = (gamma_ratio - 1.0) * (fields[:, 4] - kinetic)
    sound = jnp.sqrt(gamma_ratio * pressure * inverse)
    speeds = (jnp.abs(fields[:, 1]) + jnp.abs(fields[:, 2]) + jnp.abs(fields[:, 3])) * inverse
    return courant / (speeds + 3.0 * sound + frequency * number / 2.0)

def periodic(field_block):
    return jnp.concatenate([field_block[..., -2:], field_block, field_block[..., :2]], axis=-1)

def reference(state, donor_block, donor_offset):
    number = state.shape[0]
    indices = jnp.arange(number, dtype=jnp.int32)
    matrix = spectral_weights(indices[:, None], indices[None, :], number)
    spectral = jnp.tensordot(matrix, state, axes=(1, 0), precision=highest)

    def one_instance(packed):
        fields, time_term, blocks_of, offsets_of = packed
        rotor = fields[0]
        stator = fields[1]
        total_k = rotor.shape[3]
        positions = jnp.arange(total_k, dtype=jnp.int32)
        owner = positions // CK
        local_pos = jnp.mod(positions, CK)
        rotor_index = jnp.mod(jnp.take(blocks_of[0], owner) * CK + jnp.take(offsets_of[0], owner) + local_pos, total_k).astype(jnp.int32)
        stator_index = jnp.mod(jnp.take(blocks_of[1], owner) * CK + jnp.take(offsets_of[1], owner) + local_pos, total_k).astype(jnp.int32)
        rotor_high = jnp.take(stator[:, 0:2], rotor_index, axis=3)
        stator_low = jnp.take(rotor[:, -2:], stator_index, axis=3)
        rotor_low = jnp.concatenate([rotor[:, 0:1], rotor[:, 0:1]], axis=1)
        stator_high = jnp.concatenate([stator[:, -1:], stator[:, -1:]], axis=1)
        rotor_res = row_residual(rotor, rotor_low, rotor_high, periodic(rotor))
        stator_res = row_residual(stator, stator_low, stator_high, periodic(stator))
        residual = jnp.stack([rotor_res, stator_res]) + time_term
        step = local_step(fields, number)
        return (residual, fields - step[:, None] * residual)
    return lax.map(one_instance, (state, spectral, donor_block, donor_offset))
```

```python
import jax
import jax.numpy as jnp
from jax import lax
from jax.sharding import PartitionSpec as P

gamma_ratio = 1.4
second_coef = 0.5
fourth_coef = 1.0 / 32.0
courant = 0.8
frequency = 0.5
highest = lax.Precision.HIGHEST


def padded_2(block, sides, width):
    for axis, dim in sides:
        count = lax.axis_size(axis)
        forward = [(i, i + 1) for i in range(count - 1)]
        forward.append((count - 1, 0))
        backward = [(target, source) for source, target in forward]
        low = lax.ppermute(
            lax.slice_in_dim(block, block.shape[dim] - width, None, axis=dim), axis, forward
        )
        high = lax.ppermute(lax.slice_in_dim(block, 0, width, axis=dim), axis, backward)
        block = jnp.concatenate([low, block, high], axis=dim)
    return block


def spectral_weights(target, source, number):
    distance = jnp.mod(target - source, number)
    angle = jnp.pi / number * distance.astype(jnp.float32)
    parity = 1.0 - 2.0 * jnp.mod(distance, 2).astype(jnp.float32)
    nonzero = distance != 0
    sine_safe = jnp.where(nonzero, jnp.sin(angle), 1.0)
    cotangent = jnp.where(nonzero, jnp.cos(angle) / sine_safe, 0.0)
    return parity * (0.25 * frequency + 0.5 * frequency * cotangent)


def take_range(array, begin, length, along):
    return lax.slice_in_dim(array, begin, begin + length, axis=along)


def flux_divergence(extended, along):
    length = extended.shape[along] - 4
    cell_axis = along - 1
    density = extended[0]
    inverse = 1.0 / density
    normal_vel = extended[along] * inverse
    kinetic = 0.5 * (extended[1] ** 2 + extended[2] ** 2 + extended[3] ** 2) * inverse
    pressure = (gamma_ratio - 1.0) * (extended[4] - kinetic)
    sound = jnp.sqrt(gamma_ratio * pressure * inverse)
    momentum_flux = []
    for component in (1, 2, 3):
        if component == along:
            momentum_flux.append(extended[component] * normal_vel + pressure)
        else:
            momentum_flux.append(extended[component] * normal_vel)
    fluxes = jnp.stack(
        [extended[along]]
        + momentum_flux
        + [(extended[4] + pressure) * normal_vel, extended[5] * normal_vel]
    )
    radius = jnp.abs(normal_vel) + sound
    p_plus = take_range(pressure, 2, length + 2, cell_axis)
    p_here = take_range(pressure, 1, length + 2, cell_axis)
    p_minus = take_range(pressure, 0, length + 2, cell_axis)
    sensor = jnp.abs(p_plus - 2.0 * p_here + p_minus) / (p_plus + 2.0 * p_here + p_minus)
    spread = 0.5 * (
        take_range(radius, 1, length + 1, cell_axis) + take_range(radius, 2, length + 1, cell_axis)
    )
    eps_two = second_coef * jnp.maximum(
        take_range(sensor, 0, length + 1, cell_axis), take_range(sensor, 1, length + 1, cell_axis)
    )
    eps_four = jnp.maximum(0.0, fourth_coef - eps_two)
    first_diff = take_range(extended, 2, length + 1, along) - take_range(
        extended, 1, length + 1, along
    )
    third_diff = (
        take_range(extended, 3, length + 1, along)
        - 3.0 * take_range(extended, 2, length + 1, along)
        + 3.0 * take_range(extended, 1, length + 1, along)
        - take_range(extended, 0, length + 1, along)
    )
    interface = 0.5 * (
        take_range(fluxes, 1, length + 1, along) + take_range(fluxes, 2, length + 1, along)
    ) - spread * (eps_two * first_diff - eps_four * third_diff)
    return take_range(interface, 1, length, along) - take_range(interface, 0, length, along)


def wall_extend(block):
    mirror_sign = jnp.array([1.0, 1.0, -1.0, 1.0, 1.0, 1.0], jnp.float32).reshape(6, 1, 1, 1)
    lower_ghost = block[:, :, 0:2][:, :, ::-1] * mirror_sign
    upper_ghost = block[:, :, -2:][:, :, ::-1] * mirror_sign
    return jnp.concatenate([lower_ghost, block, upper_ghost], axis=2)


def row_residual(block, low_ghost, high_ghost, circum_ext):
    axial_ext = jnp.concatenate([low_ghost, block, high_ghost], axis=1)
    return (
        flux_divergence(axial_ext, 1)
        + flux_divergence(wall_extend(block), 2)
        + flux_divergence(circum_ext, 3)
    )


def local_step(fields, number):
    inverse = 1.0 / fields[:, 0]
    kinetic = 0.5 * (fields[:, 1] ** 2 + fields[:, 2] ** 2 + fields[:, 3] ** 2) * inverse
    pressure = (gamma_ratio - 1.0) * (fields[:, 4] - kinetic)
    sound = jnp.sqrt(gamma_ratio * pressure * inverse)
    speeds = (jnp.abs(fields[:, 1]) + jnp.abs(fields[:, 2]) + jnp.abs(fields[:, 3])) * inverse
    return courant / (speeds + 3.0 * sound + frequency * number / 2.0)


def shifted(block, axis, shift):
    count = lax.axis_size(axis)
    pairs = [(source, (source - shift) % count) for source in range(count)]
    return lax.ppermute(block, axis, pairs)


def pick(candidates, index):
    return lax.dynamic_index_in_dim(jnp.stack(candidates), index, 0, keepdims=False)


def donor_windows(faces, rotations, offsets, width):
    total_blocks = lax.axis_size("blk")
    radix = 4
    near = [faces] + [shifted(faces, "blk", s) for s in range(1, radix + 1)]
    windows = []
    for t in range(faces.shape[0]):
        low = jnp.mod(rotations[t], radix)
        first = pick([c[t] for c in near], low)
        second = pick([c[t] for c in near], low + 1)
        joined = jnp.concatenate([first, second], axis=-1)
        windows.append(lax.dynamic_slice_in_dim(joined, offsets[t], width, axis=-1))
    windows = jnp.stack(windows)
    far = [windows] + [
        shifted(windows, "blk", radix * m) for m in range(1, total_blocks // radix)
    ]
    return [pick([c[t] for c in far], rotations[t] // radix) for t in range(faces.shape[0])]


def per_device(state, donor_block, donor_offset):
    number = lax.axis_size("inst")
    total_blocks = lax.axis_size("blk")
    own_instance = lax.axis_index("inst")
    fields = state[0]
    width = fields.shape[-1]
    padded = padded_2(state, (("blk", 5),), 2)[0]
    own_block = lax.axis_index("blk")
    faces = jnp.stack([fields[1, :, 0:2], fields[0, :, -2:]])
    rotations = [jnp.mod(donor_block[0, t, 0] - own_block, total_blocks) for t in range(2)]
    offsets = [donor_offset[0, t, 0] for t in range(2)]
    rotor_high, stator_low = donor_windows(faces, rotations, offsets, width)
    piece = lax.all_gather(state, "inst", axis=0, tiled=True)
    sources = jnp.arange(piece.shape[0], dtype=jnp.int32)
    weights = spectral_weights(own_instance, sources, number)
    spectral = jnp.tensordot(weights, piece, axes=(0, 0), precision=highest)
    rotor = fields[0]
    stator = fields[1]
    rotor_low = jnp.concatenate([rotor[:, 0:1], rotor[:, 0:1]], axis=1)
    stator_high = jnp.concatenate([stator[:, -1:], stator[:, -1:]], axis=1)
    rotor_res = row_residual(rotor, rotor_low, rotor_high, padded[0])
    stator_res = row_residual(stator, stator_low, stator_high, padded[1])
    residual = jnp.stack([rotor_res, stator_res]) + spectral
    step = local_step(fields, number)
    updated = fields - step[:, None] * residual
    return (residual[None], updated[None])


def solution(mesh):
    return jax.shard_map(
        per_device,
        mesh=mesh,
        in_specs=(
            P("inst", None, None, None, None, "blk"),
            P("inst", None, "blk"),
            P("inst", None, "blk"),
        ),
        out_specs=(
            P("inst", None, None, None, None, "blk"),
            P("inst", None, None, None, None, "blk"),
        ),
        check_vma=False,
    )
```

```python
import jax
import jax.numpy as jnp
from jax import lax
from jax.sharding import PartitionSpec as P

gamma_ratio = 1.4
second_coef = 0.5
fourth_coef = 1.0 / 32.0
courant = 0.8
frequency = 0.5
highest = lax.Precision.HIGHEST


def spectral_weights(target, source, number):
    distance = jnp.mod(target - source, number)
    angle = jnp.pi / number * distance.astype(jnp.float32)
    parity = 1.0 - 2.0 * jnp.mod(distance, 2).astype(jnp.float32)
    nonzero = distance != 0
    sine_safe = jnp.where(nonzero, jnp.sin(angle), 1.0)
    cotangent = jnp.where(nonzero, jnp.cos(angle) / sine_safe, 0.0)
    return parity * (0.25 * frequency + 0.5 * frequency * cotangent)


def take_range(array, begin, length, along):
    return lax.slice_in_dim(array, begin, begin + length, axis=along)


def flux_divergence(extended, along):
    length = extended.shape[along] - 4
    cell_axis = along - 1
    density = extended[0]
    inverse = 1.0 / density
    normal_vel = extended[along] * inverse
    kinetic = 0.5 * (extended[1] ** 2 + extended[2] ** 2 + extended[3] ** 2) * inverse
    pressure = (gamma_ratio - 1.0) * (extended[4] - kinetic)
    sound = jnp.sqrt(gamma_ratio * pressure * inverse)
    momentum_flux = []
    for component in (1, 2, 3):
        if component == along:
            momentum_flux.append(extended[component] * normal_vel + pressure)
        else:
            momentum_flux.append(extended[component] * normal_vel)
    fluxes = jnp.stack(
        [extended[along]]
        + momentum_flux
        + [(extended[4] + pressure) * normal_vel, extended[5] * normal_vel]
    )
    radius = jnp.abs(normal_vel) + sound
    p_plus = take_range(pressure, 2, length + 2, cell_axis)
    p_here = take_range(pressure, 1, length + 2, cell_axis)
    p_minus = take_range(pressure, 0, length + 2, cell_axis)
    sensor = jnp.abs(p_plus - 2.0 * p_here + p_minus) / (p_plus + 2.0 * p_here + p_minus)
    spread = 0.5 * (
        take_range(radius, 1, length + 1, cell_axis) + take_range(radius, 2, length + 1, cell_axis)
    )
    eps_two = second_coef * jnp.maximum(
        take_range(sensor, 0, length + 1, cell_axis), take_range(sensor, 1, length + 1, cell_axis)
    )
    eps_four = jnp.maximum(0.0, fourth_coef - eps_two)
    first_diff = take_range(extended, 2, length + 1, along) - take_range(
        extended, 1, length + 1, along
    )
    third_diff = (
        take_range(extended, 3, length + 1, along)
        - 3.0 * take_range(extended, 2, length + 1, along)
        + 3.0 * take_range(extended, 1, length + 1, along)
        - take_range(extended, 0, length + 1, along)
    )
    interface = 0.5 * (
        take_range(fluxes, 1, length + 1, along) + take_range(fluxes, 2, length + 1, along)
    ) - spread * (eps_two * first_diff - eps_four * third_diff)
    return take_range(interface, 1, length, along) - take_range(interface, 0, length, along)


def wall_extend(block):
    mirror_sign = jnp.array([1.0, 1.0, -1.0, 1.0, 1.0, 1.0], jnp.float32).reshape(6, 1, 1, 1)
    lower_ghost = block[:, :, 0:2][:, :, ::-1] * mirror_sign
    upper_ghost = block[:, :, -2:][:, :, ::-1] * mirror_sign
    return jnp.concatenate([lower_ghost, block, upper_ghost], axis=2)


def row_residual(block, low_ghost, high_ghost, circum_ext):
    axial_ext = jnp.concatenate([low_ghost, block, high_ghost], axis=1)
    return (
        flux_divergence(axial_ext, 1)
        + flux_divergence(wall_extend(block), 2)
        + flux_divergence(circum_ext, 3)
    )


def local_step(fields, number):
    inverse = 1.0 / fields[:, 0]
    kinetic = 0.5 * (fields[:, 1] ** 2 + fields[:, 2] ** 2 + fields[:, 3] ** 2) * inverse
    pressure = (gamma_ratio - 1.0) * (fields[:, 4] - kinetic)
    sound = jnp.sqrt(gamma_ratio * pressure * inverse)
    speeds = (jnp.abs(fields[:, 1]) + jnp.abs(fields[:, 2]) + jnp.abs(fields[:, 3])) * inverse
    return courant / (speeds + 3.0 * sound + frequency * number / 2.0)


def shifted(payloads, shift):
    count = lax.axis_size("blk")
    pairs = [(source, (source - shift) % count) for source in range(count)]
    rows = [p.reshape(-1, 128) for p in payloads]
    sizes = [r.shape[0] for r in rows]
    moved = lax.ppermute(jnp.concatenate(rows, axis=0) if len(rows) > 1 else rows[0], "blk", pairs)
    pieces, begin = [], 0
    for p, size in zip(payloads, sizes):
        pieces.append(moved[begin:begin + size].reshape(p.shape))
        begin += size
    return pieces


def pick(candidates, index):
    return lax.dynamic_index_in_dim(jnp.stack(candidates), index, 0, keepdims=False)


def signed_digit(value, radix):
    return jnp.mod(value + 1, radix) - 1


def per_device(state, donor_block, donor_offset):
    number = lax.axis_size("inst")
    total_blocks = lax.axis_size("blk")
    own_instance = lax.axis_index("inst")
    own_block = lax.axis_index("blk")
    fields = state[0]
    width = fields.shape[-1]
    faces = jnp.stack([fields[1, :, 0:2], fields[0, :, -2:]])
    faces_below, halo_low = shifted([faces, fields[..., -2:]], -1)
    faces_above, halo_high = shifted([faces, fields[..., :2]], 1)
    near = [faces_below, faces, faces_above] + [shifted([faces], s)[0] for s in (2, 3)]
    padded = jnp.concatenate([halo_low, fields, halo_high], axis=-1)
    windows, far_digit, top_digit = [], [], []
    for t in range(2):
        rotation = jnp.mod(donor_block[0, t, 0] - own_block, total_blocks)
        low = signed_digit(rotation, 4)
        rest = jnp.mod((rotation - low) // 4, total_blocks // 4)
        far_digit.append(signed_digit(rest, 4))
        top_digit.append(jnp.mod((rest - far_digit[t]) // 4, 2))
        first = pick([c[t] for c in near], low + 1)
        second = pick([c[t] for c in near], low + 2)
        joined = jnp.concatenate([first, second], axis=-1)
        windows.append(lax.dynamic_slice_in_dim(joined, donor_offset[0, t, 0], width, axis=-1))
    windows = jnp.stack(windows)
    far = [shifted([windows], -4)[0], windows] + [shifted([windows], s)[0] for s in (4, 8)]
    windows = jnp.stack([pick([c[t] for c in far], far_digit[t] + 1) for t in range(2)])
    top = shifted([windows], 16)[0]
    rotor_high, stator_low = [jnp.where(top_digit[t] == 1, top[t], windows[t]) for t in range(2)]
    piece = lax.all_gather(state, "inst", axis=0, tiled=True)
    sources = jnp.arange(piece.shape[0], dtype=jnp.int32)
    weights = spectral_weights(own_instance, sources, number)
    spectral = jnp.tensordot(weights, piece, axes=(0, 0), precision=highest)
    rotor = fields[0]
    stator = fields[1]
    rotor_low = jnp.concatenate([rotor[:, 0:1], rotor[:, 0:1]], axis=1)
    stator_high = jnp.concatenate([stator[:, -1:], stator[:, -1:]], axis=1)
    rotor_res = row_residual(rotor, rotor_low, rotor_high, padded[0])
    stator_res = row_residual(stator, stator_low, stator_high, padded[1])
    residual = jnp.stack([rotor_res, stator_res]) + spectral
    step = local_step(fields, number)
    updated = fields - step[:, None] * residual
    return (residual[None], updated[None])


def solution(mesh):
    return jax.shard_map(
        per_device,
        mesh=mesh,
        in_specs=(
            P("inst", None, None, None, None, "blk"),
            P("inst", None, "blk"),
            P("inst", None, "blk"),
        ),
        out_specs=(
            P("inst", None, None, None, None, "blk"),
            P("inst", None, None, None, None, "blk"),
        ),
        check_vma=False,
    )
```

```python
import jax
import jax.numpy as jnp
from jax import lax
from jax.sharding import PartitionSpec as P

gamma_ratio = 1.4
second_coef = 0.5
fourth_coef = 1.0 / 32.0
courant = 0.8
frequency = 0.5


def spectral_weights(target, source, number):
    distance = jnp.mod(target - source, number)
    angle = jnp.pi / number * distance.astype(jnp.float32)
    parity = 1.0 - 2.0 * jnp.mod(distance, 2).astype(jnp.float32)
    nonzero = distance != 0
    sine_safe = jnp.where(nonzero, jnp.sin(angle), 1.0)
    cotangent = jnp.where(nonzero, jnp.cos(angle) / sine_safe, 0.0)
    return parity * (0.25 * frequency + 0.5 * frequency * cotangent)


def take_range(array, begin, length, along):
    return lax.slice_in_dim(array, begin, begin + length, axis=along)


def flux_divergence(extended, along):
    length = extended.shape[along] - 4
    cell_axis = along - 1
    density = extended[0]
    inverse = 1.0 / density
    normal_vel = extended[along] * inverse
    kinetic = 0.5 * (extended[1] ** 2 + extended[2] ** 2 + extended[3] ** 2) * inverse
    pressure = (gamma_ratio - 1.0) * (extended[4] - kinetic)
    sound = jnp.sqrt(gamma_ratio * pressure * inverse)
    momentum_flux = []
    for component in (1, 2, 3):
        if component == along:
            momentum_flux.append(extended[component] * normal_vel + pressure)
        else:
            momentum_flux.append(extended[component] * normal_vel)
    fluxes = jnp.stack(
        [extended[along]]
        + momentum_flux
        + [(extended[4] + pressure) * normal_vel, extended[5] * normal_vel]
    )
    radius = jnp.abs(normal_vel) + sound
    p_plus = take_range(pressure, 2, length + 2, cell_axis)
    p_here = take_range(pressure, 1, length + 2, cell_axis)
    p_minus = take_range(pressure, 0, length + 2, cell_axis)
    sensor = jnp.abs(p_plus - 2.0 * p_here + p_minus) / (p_plus + 2.0 * p_here + p_minus)
    spread = 0.5 * (
        take_range(radius, 1, length + 1, cell_axis) + take_range(radius, 2, length + 1, cell_axis)
    )
    eps_two = second_coef * jnp.maximum(
        take_range(sensor, 0, length + 1, cell_axis), take_range(sensor, 1, length + 1, cell_axis)
    )
    eps_four = jnp.maximum(0.0, fourth_coef - eps_two)
    first_diff = take_range(extended, 2, length + 1, along) - take_range(
        extended, 1, length + 1, along
    )
    third_diff = (
        take_range(extended, 3, length + 1, along)
        - 3.0 * take_range(extended, 2, length + 1, along)
        + 3.0 * take_range(extended, 1, length + 1, along)
        - take_range(extended, 0, length + 1, along)
    )
    interface = 0.5 * (
        take_range(fluxes, 1, length + 1, along) + take_range(fluxes, 2, length + 1, along)
    ) - spread * (eps_two * first_diff - eps_four * third_diff)
    return take_range(interface, 1, length, along) - take_range(interface, 0, length, along)


def wall_extend(block):
    mirror_sign = jnp.array([1.0, 1.0, -1.0, 1.0, 1.0, 1.0], jnp.float32).reshape(6, 1, 1, 1)
    lower_ghost = block[:, :, 0:2][:, :, ::-1] * mirror_sign
    upper_ghost = block[:, :, -2:][:, :, ::-1] * mirror_sign
    return jnp.concatenate([lower_ghost, block, upper_ghost], axis=2)


def row_residual(block, low_ghost, high_ghost, circum_ext):
    axial_ext = jnp.concatenate([low_ghost, block, high_ghost], axis=1)
    return (
        flux_divergence(axial_ext, 1)
        + flux_divergence(wall_extend(block), 2)
        + flux_divergence(circum_ext, 3)
    )


def local_step(fields, number):
    inverse = 1.0 / fields[:, 0]
    kinetic = 0.5 * (fields[:, 1] ** 2 + fields[:, 2] ** 2 + fields[:, 3] ** 2) * inverse
    pressure = (gamma_ratio - 1.0) * (fields[:, 4] - kinetic)
    sound = jnp.sqrt(gamma_ratio * pressure * inverse)
    speeds = (jnp.abs(fields[:, 1]) + jnp.abs(fields[:, 2]) + jnp.abs(fields[:, 3])) * inverse
    return courant / (speeds + 3.0 * sound + frequency * number / 2.0)


def shifted(payloads, shift):
    count = lax.axis_size("blk")
    pairs = [(source, (source - shift) % count) for source in range(count)]
    rows = [p.reshape(-1, 128) for p in payloads]
    sizes = [r.shape[0] for r in rows]
    moved = lax.ppermute(jnp.concatenate(rows, axis=0) if len(rows) > 1 else rows[0], "blk", pairs)
    pieces, begin = [], 0
    for p, size in zip(payloads, sizes):
        pieces.append(moved[begin:begin + size].reshape(p.shape))
        begin += size
    return pieces


def per_device(state, donor_block, donor_offset):
    number = lax.axis_size("inst")
    total_blocks = lax.axis_size("blk")
    own_instance = lax.axis_index("inst")
    own_block = lax.axis_index("blk")
    fields = state[0]
    width = fields.shape[-1]
    faces = jnp.stack([fields[1, :, 0:2], fields[0, :, -2:]])
    (halo_low,) = shifted([fields[..., -2:]], -1)
    faces_above, halo_high = shifted([faces, fields[..., :2]], 1)
    padded = jnp.concatenate([halo_low, fields, halo_high], axis=-1)
    rotations = [jnp.mod(donor_block[0, t, 0] - own_block, total_blocks) for t in range(2)]
    windows = jnp.stack([
        lax.dynamic_slice_in_dim(
            jnp.concatenate([faces[t], faces_above[t]], axis=-1), donor_offset[0, t, 0], width, axis=-1
        )
        for t in range(2)
    ])
    for k in range((total_blocks - 1).bit_length()):
        moved = shifted([windows], 1 << k)[0]
        windows = jnp.stack([
            jnp.where(jnp.bitwise_and(rotations[t] >> k, 1) == 1, moved[t], windows[t])
            for t in range(2)
        ])
    rotor_high, stator_low = windows[0], windows[1]
    piece = lax.all_gather(state, "inst", axis=0, tiled=True)
    sources = jnp.arange(piece.shape[0], dtype=jnp.int32)
    weights = spectral_weights(own_instance, sources, number)
    spectral = jnp.sum(weights.reshape((-1,) + (1,) * (piece.ndim - 1)) * piece, axis=0)
    rotor = fields[0]
    stator = fields[1]
    rotor_low = jnp.concatenate([rotor[:, 0:1], rotor[:, 0:1]], axis=1)
    stator_high = jnp.concatenate([stator[:, -1:], stator[:, -1:]], axis=1)
    rotor_res = row_residual(rotor, rotor_low, rotor_high, padded[0])
    stator_res = row_residual(stator, stator_low, stator_high, padded[1])
    step = local_step(fields, number)
    residual = jnp.stack([rotor_res, stator_res]) + spectral
    updated = fields - step[:, None] * residual
    return (residual[None], updated[None])


def solution(mesh):
    return jax.shard_map(
        per_device,
        mesh=mesh,
        in_specs=(
            P("inst", None, None, None, None, "blk"),
            P("inst", None, "blk"),
            P("inst", None, "blk"),
        ),
        out_specs=(
            P("inst", None, None, None, None, "blk"),
            P("inst", None, None, None, None, "blk"),
        ),
        check_vma=False,
    )
```

```python
import jax
import jax.numpy as jnp
from jax import lax
from jax.sharding import PartitionSpec as P

gamma_ratio = 1.4
second_coef = 0.5
fourth_coef = 1.0 / 32.0
courant = 0.8
frequency = 0.5


def spectral_weights(target, source, number):
    distance = jnp.mod(target - source, number)
    angle = jnp.pi / number * distance.astype(jnp.float32)
    parity = 1.0 - 2.0 * jnp.mod(distance, 2).astype(jnp.float32)
    nonzero = distance != 0
    sine_safe = jnp.where(nonzero, jnp.sin(angle), 1.0)
    cotangent = jnp.where(nonzero, jnp.cos(angle) / sine_safe, 0.0)
    return parity * (0.25 * frequency + 0.5 * frequency * cotangent)


def take_range(array, begin, length, along):
    return lax.slice_in_dim(array, begin, begin + length, axis=along)


def flux_divergence(extended, along):
    length = extended.shape[along] - 4
    cell_axis = along - 1
    density = extended[0]
    inverse = 1.0 / density
    normal_vel = extended[along] * inverse
    kinetic = 0.5 * (extended[1] ** 2 + extended[2] ** 2 + extended[3] ** 2) * inverse
    pressure = (gamma_ratio - 1.0) * (extended[4] - kinetic)
    sound = jnp.sqrt(gamma_ratio * pressure * inverse)
    momentum_flux = []
    for component in (1, 2, 3):
        if component == along:
            momentum_flux.append(extended[component] * normal_vel + pressure)
        else:
            momentum_flux.append(extended[component] * normal_vel)
    fluxes = jnp.stack(
        [extended[along]]
        + momentum_flux
        + [(extended[4] + pressure) * normal_vel, extended[5] * normal_vel]
    )
    radius = jnp.abs(normal_vel) + sound
    p_plus = take_range(pressure, 2, length + 2, cell_axis)
    p_here = take_range(pressure, 1, length + 2, cell_axis)
    p_minus = take_range(pressure, 0, length + 2, cell_axis)
    sensor = jnp.abs(p_plus - 2.0 * p_here + p_minus) / (p_plus + 2.0 * p_here + p_minus)
    spread = 0.5 * (
        take_range(radius, 1, length + 1, cell_axis) + take_range(radius, 2, length + 1, cell_axis)
    )
    eps_two = second_coef * jnp.maximum(
        take_range(sensor, 0, length + 1, cell_axis), take_range(sensor, 1, length + 1, cell_axis)
    )
    eps_four = jnp.maximum(0.0, fourth_coef - eps_two)
    first_diff = take_range(extended, 2, length + 1, along) - take_range(
        extended, 1, length + 1, along
    )
    third_diff = (
        take_range(extended, 3, length + 1, along)
        - 3.0 * take_range(extended, 2, length + 1, along)
        + 3.0 * take_range(extended, 1, length + 1, along)
        - take_range(extended, 0, length + 1, along)
    )
    interface = 0.5 * (
        take_range(fluxes, 1, length + 1, along) + take_range(fluxes, 2, length + 1, along)
    ) - spread * (eps_two * first_diff - eps_four * third_diff)
    return take_range(interface, 1, length, along) - take_range(interface, 0, length, along)


def wall_extend(block):
    mirror_sign = jnp.array([1.0, 1.0, -1.0, 1.0, 1.0, 1.0], jnp.float32).reshape(6, 1, 1, 1)
    lower_ghost = block[:, :, 0:2][:, :, ::-1] * mirror_sign
    upper_ghost = block[:, :, -2:][:, :, ::-1] * mirror_sign
    return jnp.concatenate([lower_ghost, block, upper_ghost], axis=2)


def row_residual(block, low_ghost, high_ghost, circum_ext):
    axial_ext = jnp.concatenate([low_ghost, block, high_ghost], axis=1)
    return (
        flux_divergence(axial_ext, 1)
        + flux_divergence(wall_extend(block), 2)
        + flux_divergence(circum_ext, 3)
    )


def local_step(fields, number):
    inverse = 1.0 / fields[:, 0]
    kinetic = 0.5 * (fields[:, 1] ** 2 + fields[:, 2] ** 2 + fields[:, 3] ** 2) * inverse
    pressure = (gamma_ratio - 1.0) * (fields[:, 4] - kinetic)
    sound = jnp.sqrt(gamma_ratio * pressure * inverse)
    speeds = (jnp.abs(fields[:, 1]) + jnp.abs(fields[:, 2]) + jnp.abs(fields[:, 3])) * inverse
    return courant / (speeds + 3.0 * sound + frequency * number / 2.0)


def shifted(payloads, shift):
    count = lax.axis_size("blk")
    pairs = [(source, (source - shift) % count) for source in range(count)]
    rows = [p.reshape(-1, 128) for p in payloads]
    sizes = [r.shape[0] for r in rows]
    moved = lax.ppermute(jnp.concatenate(rows, axis=0) if len(rows) > 1 else rows[0], "blk", pairs)
    pieces, begin = [], 0
    for p, size in zip(payloads, sizes):
        pieces.append(moved[begin:begin + size].reshape(p.shape))
        begin += size
    return pieces


def pick(candidates, index):
    chosen = candidates[0]
    for k in range(1, len(candidates)):
        chosen = jnp.where(index == k, candidates[k], chosen)
    return chosen


def signed_digit(value, radix):
    return jnp.mod(value + 1, radix) - 1


def per_device(state, donor_block, donor_offset):
    number = lax.axis_size("inst")
    total_blocks = lax.axis_size("blk")
    own_instance = lax.axis_index("inst")
    own_block = lax.axis_index("blk")
    fields = state[0]
    width = fields.shape[-1]
    faces = jnp.stack([fields[1, :, 0:2], fields[0, :, -2:]])
    rotation = jnp.mod(donor_block[0, :, 0] - own_block, total_blocks)
    low = signed_digit(rotation, 4)
    rest = jnp.mod((rotation - low) // 4, total_blocks // 4)
    far_digit = signed_digit(rest, 4)
    top_digit = jnp.mod((rest - far_digit) // 4, 2)
    offsets = donor_offset[0, :, 0]
    faces_below, halo_low = shifted([faces, fields[..., -2:]], -1)
    faces_above, halo_high = shifted([faces, fields[..., :2]], 1)
    near = [faces_below, faces, faces_above] + [shifted([faces], s)[0] for s in (2, 3)]
    padded = jnp.concatenate([halo_low, fields, halo_high], axis=-1)
    windows = []
    for t in range(2):
        first = pick([c[t] for c in near], low[t] + 1)
        second = pick([c[t] for c in near], low[t] + 2)
        joined = jnp.concatenate([first, second], axis=-1)
        windows.append(lax.dynamic_slice_in_dim(joined, offsets[t], width, axis=-1))
    windows = jnp.stack(windows)
    far = [shifted([windows], -4)[0], windows] + [shifted([windows], s)[0] for s in (4, 8)]
    windows = jnp.stack([pick([c[t] for c in far], far_digit[t] + 1) for t in range(2)])
    top = shifted([windows], 16)[0]
    rotor_high, stator_low = [jnp.where(top_digit[t] == 1, top[t], windows[t]) for t in range(2)]
    piece = lax.all_gather(state, "inst", axis=0, tiled=True)
    sources = jnp.arange(piece.shape[0], dtype=jnp.int32)
    weights = spectral_weights(own_instance, sources, number)
    spectral = jnp.sum(weights.reshape((-1,) + (1,) * (piece.ndim - 1)) * piece, axis=0)
    rotor = fields[0]
    stator = fields[1]
    rotor_low = jnp.concatenate([rotor[:, 0:1], rotor[:, 0:1]], axis=1)
    stator_high = jnp.concatenate([stator[:, -1:], stator[:, -1:]], axis=1)
    rotor_res = row_residual(rotor, rotor_low, rotor_high, padded[0])
    stator_res = row_residual(stator, stator_low, stator_high, padded[1])
    step = local_step(fields, number)
    residual = jnp.stack([rotor_res, stator_res]) + spectral
    updated = fields - step[:, None] * residual
    return (residual[None], updated[None])


def solution(mesh):
    return jax.shard_map(
        per_device,
        mesh=mesh,
        in_specs=(
            P("inst", None, None, None, None, "blk"),
            P("inst", None, "blk"),
            P("inst", None, "blk"),
        ),
        out_specs=(
            P("inst", None, None, None, None, "blk"),
            P("inst", None, None, None, None, "blk"),
        ),
        check_vma=False,
    )
```

```python
import jax
import jax.numpy as jnp
from jax import lax
from jax.sharding import PartitionSpec as P

gamma_ratio = 1.4
second_coef = 0.5
fourth_coef = 1.0 / 32.0
courant = 0.8
frequency = 0.5
highest = lax.Precision.HIGHEST


def spectral_weights(target, source, number):
    distance = jnp.mod(target - source, number)
    angle = jnp.pi / number * distance.astype(jnp.float32)
    parity = 1.0 - 2.0 * jnp.mod(distance, 2).astype(jnp.float32)
    nonzero = distance != 0
    sine_safe = jnp.where(nonzero, jnp.sin(angle), 1.0)
    cotangent = jnp.where(nonzero, jnp.cos(angle) / sine_safe, 0.0)
    return parity * (0.25 * frequency + 0.5 * frequency * cotangent)


def take_range(array, begin, length, along):
    return lax.slice_in_dim(array, begin, begin + length, axis=along)


def flux_divergence(extended, along):
    length = extended.shape[along] - 4
    cell_axis = along - 1
    density = extended[0]
    inverse = 1.0 / density
    normal_vel = extended[along] * inverse
    kinetic = 0.5 * (extended[1] ** 2 + extended[2] ** 2 + extended[3] ** 2) * inverse
    pressure = (gamma_ratio - 1.0) * (extended[4] - kinetic)
    sound = jnp.sqrt(gamma_ratio * pressure * inverse)
    momentum_flux = []
    for component in (1, 2, 3):
        if component == along:
            momentum_flux.append(extended[component] * normal_vel + pressure)
        else:
            momentum_flux.append(extended[component] * normal_vel)
    fluxes = jnp.stack(
        [extended[along]]
        + momentum_flux
        + [(extended[4] + pressure) * normal_vel, extended[5] * normal_vel]
    )
    radius = jnp.abs(normal_vel) + sound
    p_plus = take_range(pressure, 2, length + 2, cell_axis)
    p_here = take_range(pressure, 1, length + 2, cell_axis)
    p_minus = take_range(pressure, 0, length + 2, cell_axis)
    sensor = jnp.abs(p_plus - 2.0 * p_here + p_minus) / (p_plus + 2.0 * p_here + p_minus)
    spread = 0.5 * (
        take_range(radius, 1, length + 1, cell_axis) + take_range(radius, 2, length + 1, cell_axis)
    )
    eps_two = second_coef * jnp.maximum(
        take_range(sensor, 0, length + 1, cell_axis), take_range(sensor, 1, length + 1, cell_axis)
    )
    eps_four = jnp.maximum(0.0, fourth_coef - eps_two)
    first_diff = take_range(extended, 2, length + 1, along) - take_range(
        extended, 1, length + 1, along
    )
    third_diff = (
        take_range(extended, 3, length + 1, along)
        - 3.0 * take_range(extended, 2, length + 1, along)
        + 3.0 * take_range(extended, 1, length + 1, along)
        - take_range(extended, 0, length + 1, along)
    )
    interface = 0.5 * (
        take_range(fluxes, 1, length + 1, along) + take_range(fluxes, 2, length + 1, along)
    ) - spread * (eps_two * first_diff - eps_four * third_diff)
    return take_range(interface, 1, length, along) - take_range(interface, 0, length, along)


def wall_extend(block):
    mirror_sign = jnp.array([1.0, 1.0, -1.0, 1.0, 1.0, 1.0], jnp.float32).reshape(6, 1, 1, 1)
    lower_ghost = block[:, :, 0:2][:, :, ::-1] * mirror_sign
    upper_ghost = block[:, :, -2:][:, :, ::-1] * mirror_sign
    return jnp.concatenate([lower_ghost, block, upper_ghost], axis=2)


def row_residual(block, low_ghost, high_ghost, circum_ext):
    axial_ext = jnp.concatenate([low_ghost, block, high_ghost], axis=1)
    return (
        flux_divergence(axial_ext, 1)
        + flux_divergence(wall_extend(block), 2)
        + flux_divergence(circum_ext, 3)
    )


def local_step(fields, number):
    inverse = 1.0 / fields[:, 0]
    kinetic = 0.5 * (fields[:, 1] ** 2 + fields[:, 2] ** 2 + fields[:, 3] ** 2) * inverse
    pressure = (gamma_ratio - 1.0) * (fields[:, 4] - kinetic)
    sound = jnp.sqrt(gamma_ratio * pressure * inverse)
    speeds = (jnp.abs(fields[:, 1]) + jnp.abs(fields[:, 2]) + jnp.abs(fields[:, 3])) * inverse
    return courant / (speeds + 3.0 * sound + frequency * number / 2.0)


def shifted(payloads, shift):
    count = lax.axis_size("blk")
    pairs = [(source, (source - shift) % count) for source in range(count)]
    rows = [p.reshape(-1, 128) for p in payloads]
    sizes = [r.shape[0] for r in rows]
    moved = lax.ppermute(jnp.concatenate(rows, axis=0) if len(rows) > 1 else rows[0], "blk", pairs)
    pieces, begin = [], 0
    for p, size in zip(payloads, sizes):
        pieces.append(moved[begin:begin + size].reshape(p.shape))
        begin += size
    return pieces


def pick(candidates, index):
    chosen = candidates[0]
    for k in range(1, len(candidates)):
        chosen = jnp.where(index == k, candidates[k], chosen)
    return chosen


def cut_window(first, second, offset):
    width = first.shape[-1]
    joined = jnp.concatenate([first, second], axis=-1).reshape(-1, 2 * width)
    rows = lax.broadcasted_iota(jnp.int32, (2 * width, width), 0)
    cols = lax.broadcasted_iota(jnp.int32, (2 * width, width), 1)
    selection = (rows == cols + offset).astype(jnp.float32)
    return jnp.dot(joined, selection, precision=highest).reshape(first.shape)


def signed_digit(value, radix):
    return jnp.mod(value + 1, radix) - 1


def per_device(state, donor_block, donor_offset):
    number = lax.axis_size("inst")
    total_blocks = lax.axis_size("blk")
    own_instance = lax.axis_index("inst")
    own_block = lax.axis_index("blk")
    fields = state[0]
    faces = jnp.stack([fields[1, :, 0:2], fields[0, :, -2:]])
    faces_below, halo_low = shifted([faces, fields[..., -2:]], -1)
    faces_above, halo_high = shifted([faces, fields[..., :2]], 1)
    near = [faces_below, faces, faces_above] + [shifted([faces], s)[0] for s in (2, 3)]
    padded = jnp.concatenate([halo_low, fields, halo_high], axis=-1)
    windows, far_digit, top_digit = [], [], []
    for t in range(2):
        rotation = jnp.mod(donor_block[0, t, 0] - own_block, total_blocks)
        low = signed_digit(rotation, 4)
        rest = jnp.mod((rotation - low) // 4, total_blocks // 4)
        far_digit.append(signed_digit(rest, 4))
        top_digit.append(jnp.mod((rest - far_digit[t]) // 4, 2))
        first = pick([c[t] for c in near], low + 1)
        second = pick([c[t] for c in near], low + 2)
        windows.append(cut_window(first, second, donor_offset[0, t, 0]))
    windows = jnp.stack(windows)
    far = [shifted([windows], -4)[0], windows] + [shifted([windows], s)[0] for s in (4, 8)]
    windows = jnp.stack([pick([c[t] for c in far], far_digit[t] + 1) for t in range(2)])
    top = shifted([windows], 16)[0]
    rotor_high, stator_low = [jnp.where(top_digit[t] == 1, top[t], windows[t]) for t in range(2)]
    piece = lax.all_gather(state, "inst", axis=0, tiled=True)
    sources = jnp.arange(piece.shape[0], dtype=jnp.int32)
    weights = spectral_weights(own_instance, sources, number)
    spectral = jnp.sum(weights.reshape((-1,) + (1,) * (piece.ndim - 1)) * piece, axis=0)
    rotor = fields[0]
    stator = fields[1]
    rotor_low = jnp.concatenate([rotor[:, 0:1], rotor[:, 0:1]], axis=1)
    stator_high = jnp.concatenate([stator[:, -1:], stator[:, -1:]], axis=1)
    rotor_res = row_residual(rotor, rotor_low, rotor_high, padded[0])
    stator_res = row_residual(stator, stator_low, stator_high, padded[1])
    step = local_step(fields, number)
    residual = jnp.stack([rotor_res, stator_res]) + spectral
    updated = fields - step[:, None] * residual
    return (residual[None], updated[None])


def solution(mesh):
    return jax.shard_map(
        per_device,
        mesh=mesh,
        in_specs=(
            P("inst", None, None, None, None, "blk"),
            P("inst", None, "blk"),
            P("inst", None, "blk"),
        ),
        out_specs=(
            P("inst", None, None, None, None, "blk"),
            P("inst", None, None, None, None, "blk"),
        ),
        check_vma=False,
    )
```

```python
import jax
import jax.numpy as jnp
from jax import lax
from jax.sharding import PartitionSpec as P

gamma_ratio = 1.4
second_coef = 0.5
fourth_coef = 1.0 / 32.0
courant = 0.8
frequency = 0.5


def spectral_weights(target, source, number):
    distance = jnp.mod(target - source, number)
    angle = jnp.pi / number * distance.astype(jnp.float32)
    parity = 1.0 - 2.0 * jnp.mod(distance, 2).astype(jnp.float32)
    nonzero = distance != 0
    sine_safe = jnp.where(nonzero, jnp.sin(angle), 1.0)
    cotangent = jnp.where(nonzero, jnp.cos(angle) / sine_safe, 0.0)
    return parity * (0.25 * frequency + 0.5 * frequency * cotangent)


def take_range(array, begin, length, along):
    return lax.slice_in_dim(array, begin, begin + length, axis=along)


def flux_divergence(extended, along):
    length = extended.shape[along] - 4
    cell_axis = along - 1
    density = extended[0]
    inverse = 1.0 / density
    normal_vel = extended[along] * inverse
    kinetic = 0.5 * (extended[1] ** 2 + extended[2] ** 2 + extended[3] ** 2) * inverse
    pressure = (gamma_ratio - 1.0) * (extended[4] - kinetic)
    sound = jnp.sqrt(gamma_ratio * pressure * inverse)
    momentum_flux = []
    for component in (1, 2, 3):
        if component == along:
            momentum_flux.append(extended[component] * normal_vel + pressure)
        else:
            momentum_flux.append(extended[component] * normal_vel)
    fluxes = jnp.stack(
        [extended[along]]
        + momentum_flux
        + [(extended[4] + pressure) * normal_vel, extended[5] * normal_vel]
    )
    radius = jnp.abs(normal_vel) + sound
    p_plus = take_range(pressure, 2, length + 2, cell_axis)
    p_here = take_range(pressure, 1, length + 2, cell_axis)
    p_minus = take_range(pressure, 0, length + 2, cell_axis)
    sensor = jnp.abs(p_plus - 2.0 * p_here + p_minus) / (p_plus + 2.0 * p_here + p_minus)
    spread = 0.5 * (
        take_range(radius, 1, length + 1, cell_axis) + take_range(radius, 2, length + 1, cell_axis)
    )
    eps_two = second_coef * jnp.maximum(
        take_range(sensor, 0, length + 1, cell_axis), take_range(sensor, 1, length + 1, cell_axis)
    )
    eps_four = jnp.maximum(0.0, fourth_coef - eps_two)
    first_diff = take_range(extended, 2, length + 1, along) - take_range(
        extended, 1, length + 1, along
    )
    third_diff = (
        take_range(extended, 3, length + 1, along)
        - 3.0 * take_range(extended, 2, length + 1, along)
        + 3.0 * take_range(extended, 1, length + 1, along)
        - take_range(extended, 0, length + 1, along)
    )
    interface = 0.5 * (
        take_range(fluxes, 1, length + 1, along) + take_range(fluxes, 2, length + 1, along)
    ) - spread * (eps_two * first_diff - eps_four * third_diff)
    return take_range(interface, 1, length, along) - take_range(interface, 0, length, along)


def wall_extend(block):
    mirror_sign = jnp.array([1.0, 1.0, -1.0, 1.0, 1.0, 1.0], jnp.float32).reshape(6, 1, 1, 1)
    lower_ghost = block[:, :, 0:2][:, :, ::-1] * mirror_sign
    upper_ghost = block[:, :, -2:][:, :, ::-1] * mirror_sign
    return jnp.concatenate([lower_ghost, block, upper_ghost], axis=2)


def row_residual(block, low_ghost, high_ghost, circum_ext):
    axial_ext = jnp.concatenate([low_ghost, block, high_ghost], axis=1)
    return (
        flux_divergence(axial_ext, 1)
        + flux_divergence(wall_extend(block), 2)
        + flux_divergence(circum_ext, 3)
    )


def local_step(fields, number):
    inverse = 1.0 / fields[:, 0]
    kinetic = 0.5 * (fields[:, 1] ** 2 + fields[:, 2] ** 2 + fields[:, 3] ** 2) * inverse
    pressure = (gamma_ratio - 1.0) * (fields[:, 4] - kinetic)
    sound = jnp.sqrt(gamma_ratio * pressure * inverse)
    speeds = (jnp.abs(fields[:, 1]) + jnp.abs(fields[:, 2]) + jnp.abs(fields[:, 3])) * inverse
    return courant / (speeds + 3.0 * sound + frequency * number / 2.0)


def shifted(payloads, shift):
    count = lax.axis_size("blk")
    pairs = [(source, (source - shift) % count) for source in range(count)]
    rows = [p.reshape(-1, 128) for p in payloads]
    sizes = [r.shape[0] for r in rows]
    moved = lax.ppermute(jnp.concatenate(rows, axis=0) if len(rows) > 1 else rows[0], "blk", pairs)
    pieces, begin = [], 0
    for p, size in zip(payloads, sizes):
        pieces.append(moved[begin:begin + size].reshape(p.shape))
        begin += size
    return pieces


def pick(candidates, index):
    return lax.dynamic_index_in_dim(jnp.stack(candidates), index, 0, keepdims=False)


def signed_digit(value, radix):
    return jnp.mod(value + 1, radix) - 1


def per_device(state, donor_block, donor_offset):
    number = lax.axis_size("inst")
    total_blocks = lax.axis_size("blk")
    own_instance = lax.axis_index("inst")
    own_block = lax.axis_index("blk")
    fields = state[0]
    width = fields.shape[-1]
    faces = jnp.stack([fields[1, :, 0:2], fields[0, :, -2:]])
    faces_below, block_below = shifted([faces, fields], -1)
    faces_above, block_above = shifted([faces, fields], 1)
    near = [faces_below, faces, faces_above] + [shifted([faces], s)[0] for s in (2, 3)]
    padded = jnp.concatenate([block_below[..., -2:], fields, block_above[..., :2]], axis=-1)
    windows, far_digit, top_digit = [], [], []
    for t in range(2):
        rotation = jnp.mod(donor_block[0, t, 0] - own_block, total_blocks)
        low = signed_digit(rotation, 4)
        rest = jnp.mod((rotation - low) // 4, total_blocks // 4)
        far_digit.append(signed_digit(rest, 4))
        top_digit.append(jnp.mod((rest - far_digit[t]) // 4, 2))
        first = pick([c[t] for c in near], low + 1)
        second = pick([c[t] for c in near], low + 2)
        joined = jnp.concatenate([first, second], axis=-1)
        windows.append(lax.dynamic_slice_in_dim(joined, donor_offset[0, t, 0], width, axis=-1))
    windows = jnp.stack(windows)
    far = [shifted([windows], -4)[0], windows] + [shifted([windows], s)[0] for s in (4, 8)]
    windows = jnp.stack([pick([c[t] for c in far], far_digit[t] + 1) for t in range(2)])
    top = shifted([windows], 16)[0]
    rotor_high, stator_low = [jnp.where(top_digit[t] == 1, top[t], windows[t]) for t in range(2)]
    piece = lax.all_gather(state, "inst", axis=0, tiled=True)
    sources = jnp.arange(piece.shape[0], dtype=jnp.int32)
    weights = spectral_weights(own_instance, sources, number)
    spectral = jnp.sum(weights.reshape((-1,) + (1,) * (piece.ndim - 1)) * piece, axis=0)
    rotor = fields[0]
    stator = fields[1]
    rotor_low = jnp.concatenate([rotor[:, 0:1], rotor[:, 0:1]], axis=1)
    stator_high = jnp.concatenate([stator[:, -1:], stator[:, -1:]], axis=1)
    rotor_res = row_residual(rotor, rotor_low, rotor_high, padded[0])
    stator_res = row_residual(stator, stator_low, stator_high, padded[1])
    step = local_step(fields, number)
    residual = jnp.stack([rotor_res, stator_res]) + spectral
    updated = fields - step[:, None] * residual
    return (residual[None], updated[None])


def solution(mesh):
    return jax.shard_map(
        per_device,
        mesh=mesh,
        in_specs=(
            P("inst", None, None, None, None, "blk"),
            P("inst", None, "blk"),
            P("inst", None, "blk"),
        ),
        out_specs=(
            P("inst", None, None, None, None, "blk"),
            P("inst", None, None, None, None, "blk"),
        ),
        check_vma=False,
    )
```

```python
import jax
import jax.numpy as jnp
from jax import lax
from jax.sharding import PartitionSpec as P

gamma_ratio = 1.4
second_coef = 0.5
fourth_coef = 1.0 / 32.0
courant = 0.8
frequency = 0.5
highest = lax.Precision.HIGHEST


def spectral_weights(target, source, number):
    distance = jnp.mod(target - source, number)
    angle = jnp.pi / number * distance.astype(jnp.float32)
    parity = 1.0 - 2.0 * jnp.mod(distance, 2).astype(jnp.float32)
    nonzero = distance != 0
    sine_safe = jnp.where(nonzero, jnp.sin(angle), 1.0)
    cotangent = jnp.where(nonzero, jnp.cos(angle) / sine_safe, 0.0)
    return parity * (0.25 * frequency + 0.5 * frequency * cotangent)


def take_range(array, begin, length, along):
    return lax.slice_in_dim(array, begin, begin + length, axis=along)


def flux_divergence(extended, along):
    length = extended.shape[along] - 4
    cell_axis = along - 1
    density = extended[0]
    inverse = 1.0 / density
    normal_vel = extended[along] * inverse
    kinetic = 0.5 * (extended[1] ** 2 + extended[2] ** 2 + extended[3] ** 2) * inverse
    pressure = (gamma_ratio - 1.0) * (extended[4] - kinetic)
    sound = jnp.sqrt(gamma_ratio * pressure * inverse)
    momentum_flux = []
    for component in (1, 2, 3):
        if component == along:
            momentum_flux.append(extended[component] * normal_vel + pressure)
        else:
            momentum_flux.append(extended[component] * normal_vel)
    fluxes = jnp.stack(
        [extended[along]]
        + momentum_flux
        + [(extended[4] + pressure) * normal_vel, extended[5] * normal_vel]
    )
    radius = jnp.abs(normal_vel) + sound
    p_plus = take_range(pressure, 2, length + 2, cell_axis)
    p_here = take_range(pressure, 1, length + 2, cell_axis)
    p_minus = take_range(pressure, 0, length + 2, cell_axis)
    sensor = jnp.abs(p_plus - 2.0 * p_here + p_minus) / (p_plus + 2.0 * p_here + p_minus)
    spread = 0.5 * (
        take_range(radius, 1, length + 1, cell_axis) + take_range(radius, 2, length + 1, cell_axis)
    )
    eps_two = second_coef * jnp.maximum(
        take_range(sensor, 0, length + 1, cell_axis), take_range(sensor, 1, length + 1, cell_axis)
    )
    eps_four = jnp.maximum(0.0, fourth_coef - eps_two)
    first_diff = take_range(extended, 2, length + 1, along) - take_range(
        extended, 1, length + 1, along
    )
    third_diff = (
        take_range(extended, 3, length + 1, along)
        - 3.0 * take_range(extended, 2, length + 1, along)
        + 3.0 * take_range(extended, 1, length + 1, along)
        - take_range(extended, 0, length + 1, along)
    )
    interface = 0.5 * (
        take_range(fluxes, 1, length + 1, along) + take_range(fluxes, 2, length + 1, along)
    ) - spread * (eps_two * first_diff - eps_four * third_diff)
    return take_range(interface, 1, length, along) - take_range(interface, 0, length, along)


def wall_extend(block):
    mirror_sign = jnp.array([1.0, 1.0, -1.0, 1.0, 1.0, 1.0], jnp.float32).reshape(6, 1, 1, 1)
    lower_ghost = block[:, :, 0:2][:, :, ::-1] * mirror_sign
    upper_ghost = block[:, :, -2:][:, :, ::-1] * mirror_sign
    return jnp.concatenate([lower_ghost, block, upper_ghost], axis=2)


def row_residual(block, low_ghost, high_ghost, circum_ext):
    axial_ext = jnp.concatenate([low_ghost, block, high_ghost], axis=1)
    return (
        flux_divergence(axial_ext, 1)
        + flux_divergence(wall_extend(block), 2)
        + flux_divergence(circum_ext, 3)
    )


def local_step(fields, number):
    inverse = 1.0 / fields[:, 0]
    kinetic = 0.5 * (fields[:, 1] ** 2 + fields[:, 2] ** 2 + fields[:, 3] ** 2) * inverse
    pressure = (gamma_ratio - 1.0) * (fields[:, 4] - kinetic)
    sound = jnp.sqrt(gamma_ratio * pressure * inverse)
    speeds = (jnp.abs(fields[:, 1]) + jnp.abs(fields[:, 2]) + jnp.abs(fields[:, 3])) * inverse
    return courant / (speeds + 3.0 * sound + frequency * number / 2.0)


def shifted(payloads, shift):
    count = lax.axis_size("blk")
    pairs = [(source, (source - shift) % count) for source in range(count)]
    rows = [p.reshape(-1, 128) for p in payloads]
    sizes = [r.shape[0] for r in rows]
    moved = lax.ppermute(jnp.concatenate(rows, axis=0) if len(rows) > 1 else rows[0], "blk", pairs)
    pieces, begin = [], 0
    for p, size in zip(payloads, sizes):
        pieces.append(moved[begin:begin + size].reshape(p.shape))
        begin += size
    return pieces


def pick(candidates, index):
    chosen = candidates[0]
    for k in range(1, len(candidates)):
        chosen = jnp.where(index == k, candidates[k], chosen)
    return chosen


def cut_window(first, second, offset):
    width = first.shape[-1]
    joined = jnp.concatenate([first, second], axis=-1).reshape(-1, 2 * width)
    rows = lax.broadcasted_iota(jnp.int32, (2 * width, width), 0)
    cols = lax.broadcasted_iota(jnp.int32, (2 * width, width), 1)
    selection = (rows == cols + offset).astype(jnp.float32)
    return jnp.dot(joined, selection, precision=highest).reshape(first.shape)


def signed_digit(value, radix):
    return jnp.mod(value + 1, radix) - 1


def per_device(state, donor_block, donor_offset):
    number = lax.axis_size("inst")
    total_blocks = lax.axis_size("blk")
    own_instance = lax.axis_index("inst")
    own_block = lax.axis_index("blk")
    fields = state[0]
    faces = jnp.stack([fields[1, :, 0:2], fields[0, :, -2:]])
    faces_below, halo_low = shifted([faces, fields[..., -2:]], -1)
    faces_above, halo_high = shifted([faces, fields[..., :2]], 1)
    near = [faces_below, faces, faces_above]
    padded = jnp.concatenate([halo_low, fields, halo_high], axis=-1)
    windows, mid_digit, top_digit = [], [], []
    for t in range(2):
        rotation = jnp.mod(donor_block[0, t, 0] - own_block, total_blocks)
        low = signed_digit(rotation, 2)
        rest = jnp.mod((rotation - low) // 2, total_blocks // 2)
        mid_digit.append(signed_digit(rest, 4))
        top_digit.append(signed_digit(jnp.mod((rest - mid_digit[t]) // 4, 4), 4))
        first = pick([c[t] for c in near], low + 1)
        second = pick([c[t] for c in near], low + 2)
        windows.append(cut_window(first, second, donor_offset[0, t, 0]))
    windows = jnp.stack(windows)
    mid = [shifted([windows], -2)[0], windows] + [shifted([windows], s)[0] for s in (2, 4)]
    windows = jnp.stack([pick([c[t] for c in mid], mid_digit[t] + 1) for t in range(2)])
    top = [shifted([windows], -8)[0], windows] + [shifted([windows], s)[0] for s in (8, 16)]
    rotor_high, stator_low = [pick([c[t] for c in top], top_digit[t] + 1) for t in range(2)]
    piece = lax.all_gather(state, "inst", axis=0, tiled=True)
    sources = jnp.arange(piece.shape[0], dtype=jnp.int32)
    weights = spectral_weights(own_instance, sources, number)
    spectral = jnp.sum(weights.reshape((-1,) + (1,) * (piece.ndim - 1)) * piece, axis=0)
    rotor = fields[0]
    stator = fields[1]
    rotor_low = jnp.concatenate([rotor[:, 0:1], rotor[:, 0:1]], axis=1)
    stator_high = jnp.concatenate([stator[:, -1:], stator[:, -1:]], axis=1)
    rotor_res = row_residual(rotor, rotor_low, rotor_high, padded[0])
    stator_res = row_residual(stator, stator_low, stator_high, padded[1])
    step = local_step(fields, number)
    residual = jnp.stack([rotor_res, stator_res]) + spectral
    updated = fields - step[:, None] * residual
    return (residual[None], updated[None])


def solution(mesh):
    return jax.shard_map(
        per_device,
        mesh=mesh,
        in_specs=(
            P("inst", None, None, None, None, "blk"),
            P("inst", None, "blk"),
            P("inst", None, "blk"),
        ),
        out_specs=(
            P("inst", None, None, None, None, "blk"),
            P("inst", None, None, None, None, "blk"),
        ),
        check_vma=False,
    )
```

```python
import jax
import jax.numpy as jnp
from jax import lax
from jax.sharding import PartitionSpec as P

gamma_ratio = 1.4
second_coef = 0.5
fourth_coef = 1.0 / 32.0
courant = 0.8
frequency = 0.5


def spectral_weights(target, source, number):
    distance = jnp.mod(target - source, number)
    angle = jnp.pi / number * distance.astype(jnp.float32)
    parity = 1.0 - 2.0 * jnp.mod(distance, 2).astype(jnp.float32)
    nonzero = distance != 0
    sine_safe = jnp.where(nonzero, jnp.sin(angle), 1.0)
    cotangent = jnp.where(nonzero, jnp.cos(angle) / sine_safe, 0.0)
    return parity * (0.25 * frequency + 0.5 * frequency * cotangent)


def take_range(array, begin, length, along):
    return lax.slice_in_dim(array, begin, begin + length, axis=along)


def flux_divergence(extended, along):
    length = extended.shape[along] - 4
    cell_axis = along - 1
    density = extended[0]
    inverse = 1.0 / density
    normal_vel = extended[along] * inverse
    kinetic = 0.5 * (extended[1] ** 2 + extended[2] ** 2 + extended[3] ** 2) * inverse
    pressure = (gamma_ratio - 1.0) * (extended[4] - kinetic)
    sound = jnp.sqrt(gamma_ratio * pressure * inverse)
    momentum_flux = []
    for component in (1, 2, 3):
        if component == along:
            momentum_flux.append(extended[component] * normal_vel + pressure)
        else:
            momentum_flux.append(extended[component] * normal_vel)
    fluxes = jnp.stack(
        [extended[along]]
        + momentum_flux
        + [(extended[4] + pressure) * normal_vel, extended[5] * normal_vel]
    )
    radius = jnp.abs(normal_vel) + sound
    p_plus = take_range(pressure, 2, length + 2, cell_axis)
    p_here = take_range(pressure, 1, length + 2, cell_axis)
    p_minus = take_range(pressure, 0, length + 2, cell_axis)
    sensor = jnp.abs(p_plus - 2.0 * p_here + p_minus) / (p_plus + 2.0 * p_here + p_minus)
    spread = 0.5 * (
        take_range(radius, 1, length + 1, cell_axis) + take_range(radius, 2, length + 1, cell_axis)
    )
    eps_two = second_coef * jnp.maximum(
        take_range(sensor, 0, length + 1, cell_axis), take_range(sensor, 1, length + 1, cell_axis)
    )
    eps_four = jnp.maximum(0.0, fourth_coef - eps_two)
    first_diff = take_range(extended, 2, length + 1, along) - take_range(
        extended, 1, length + 1, along
    )
    third_diff = (
        take_range(extended, 3, length + 1, along)
        - 3.0 * take_range(extended, 2, length + 1, along)
        + 3.0 * take_range(extended, 1, length + 1, along)
        - take_range(extended, 0, length + 1, along)
    )
    interface = 0.5 * (
        take_range(fluxes, 1, length + 1, along) + take_range(fluxes, 2, length + 1, along)
    ) - spread * (eps_two * first_diff - eps_four * third_diff)
    return take_range(interface, 1, length, along) - take_range(interface, 0, length, along)


def wall_extend(block):
    mirror_sign = jnp.array([1.0, 1.0, -1.0, 1.0, 1.0, 1.0], jnp.float32).reshape(6, 1, 1, 1)
    lower_ghost = block[:, :, 0:2][:, :, ::-1] * mirror_sign
    upper_ghost = block[:, :, -2:][:, :, ::-1] * mirror_sign
    return jnp.concatenate([lower_ghost, block, upper_ghost], axis=2)


def row_residual(block, low_ghost, high_ghost, circum_ext):
    axial_ext = jnp.concatenate([low_ghost, block, high_ghost], axis=1)
    return (
        flux_divergence(axial_ext, 1)
        + flux_divergence(wall_extend(block), 2)
        + flux_divergence(circum_ext, 3)
    )


def local_step(fields, number):
    inverse = 1.0 / fields[:, 0]
    kinetic = 0.5 * (fields[:, 1] ** 2 + fields[:, 2] ** 2 + fields[:, 3] ** 2) * inverse
    pressure = (gamma_ratio - 1.0) * (fields[:, 4] - kinetic)
    sound = jnp.sqrt(gamma_ratio * pressure * inverse)
    speeds = (jnp.abs(fields[:, 1]) + jnp.abs(fields[:, 2]) + jnp.abs(fields[:, 3])) * inverse
    return courant / (speeds + 3.0 * sound + frequency * number / 2.0)


def shifted(payloads, shift):
    count = lax.axis_size("blk")
    pairs = [(source, (source - shift) % count) for source in range(count)]
    rows = [p.reshape(-1, 128) for p in payloads]
    sizes = [r.shape[0] for r in rows]
    moved = lax.ppermute(jnp.concatenate(rows, axis=0) if len(rows) > 1 else rows[0], "blk", pairs)
    pieces, begin = [], 0
    for p, size in zip(payloads, sizes):
        pieces.append(moved[begin:begin + size].reshape(p.shape))
        begin += size
    return pieces


def pick(candidates, index):
    return lax.dynamic_index_in_dim(jnp.stack(candidates), index, 0, keepdims=False)


def signed_digit(value, radix):
    return jnp.mod(value + 1, radix) - 1


def per_device(state, donor_block, donor_offset):
    number = lax.axis_size("inst")
    total_blocks = lax.axis_size("blk")
    own_instance = lax.axis_index("inst")
    own_block = lax.axis_index("blk")
    fields = state[0]
    width = fields.shape[-1]
    faces = jnp.stack([fields[1, :, 0:2], fields[0, :, -2:]])
    faces_below, halo_low = shifted([faces, fields[..., -2:]], -1)
    faces_above, halo_high = shifted([faces, fields[..., :2]], 1)
    near = [faces_below, faces, faces_above]
    padded = jnp.concatenate([halo_low, fields, halo_high], axis=-1)
    windows, mid_digit, top_digit = [], [], []
    for t in range(2):
        rotation = jnp.mod(donor_block[0, t, 0] - own_block, total_blocks)
        low = signed_digit(rotation, 2)
        rest = jnp.mod((rotation - low) // 2, total_blocks // 2)
        mid_digit.append(signed_digit(rest, 4))
        top_digit.append(signed_digit(jnp.mod((rest - mid_digit[t]) // 4, 4), 4))
        first = pick([c[t] for c in near], low + 1)
        second = pick([c[t] for c in near], low + 2)
        joined = jnp.concatenate([first, second], axis=-1)
        windows.append(lax.dynamic_slice_in_dim(joined, donor_offset[0, t, 0], width, axis=-1))
    windows = jnp.stack(windows)
    far = [shifted([windows], -8)[0], windows] + [shifted([windows], s)[0] for s in (8, 16)]
    windows = jnp.stack([pick([c[t] for c in far], top_digit[t] + 1) for t in range(2)])
    near_last = [shifted([windows], -2)[0], windows] + [shifted([windows], s)[0] for s in (2, 4)]
    rotor_high, stator_low = [pick([c[t] for c in near_last], mid_digit[t] + 1) for t in range(2)]
    piece = lax.all_gather(state, "inst", axis=0, tiled=True)
    sources = jnp.arange(piece.shape[0], dtype=jnp.int32)
    weights = spectral_weights(own_instance, sources, number)
    spectral = jnp.sum(weights.reshape((-1,) + (1,) * (piece.ndim - 1)) * piece, axis=0)
    rotor = fields[0]
    stator = fields[1]
    rotor_low = jnp.concatenate([rotor[:, 0:1], rotor[:, 0:1]], axis=1)
    stator_high = jnp.concatenate([stator[:, -1:], stator[:, -1:]], axis=1)
    rotor_res = row_residual(rotor, rotor_low, rotor_high, padded[0])
    stator_res = row_residual(stator, stator_low, stator_high, padded[1])
    step = local_step(fields, number)
    residual = jnp.stack([rotor_res, stator_res]) + spectral
    updated = fields - step[:, None] * residual
    return (residual[None], updated[None])


def solution(mesh):
    return jax.shard_map(
        per_device,
        mesh=mesh,
        in_specs=(
            P("inst", None, None, None, None, "blk"),
            P("inst", None, "blk"),
            P("inst", None, "blk"),
        ),
        out_specs=(
            P("inst", None, None, None, None, "blk"),
            P("inst", None, None, None, None, "blk"),
        ),
        check_vma=False,
    )
```

```python
import jax
import jax.numpy as jnp
from jax import lax
from jax.sharding import PartitionSpec as P

gamma_ratio = 1.4
second_coef = 0.5
fourth_coef = 1.0 / 32.0
courant = 0.8
frequency = 0.5


def spectral_weights(target, source, number):
    distance = jnp.mod(target - source, number)
    angle = jnp.pi / number * distance.astype(jnp.float32)
    parity = 1.0 - 2.0 * jnp.mod(distance, 2).astype(jnp.float32)
    nonzero = distance != 0
    sine_safe = jnp.where(nonzero, jnp.sin(angle), 1.0)
    cotangent = jnp.where(nonzero, jnp.cos(angle) / sine_safe, 0.0)
    return parity * (0.25 * frequency + 0.5 * frequency * cotangent)


def take_range(array, begin, length, along):
    return lax.slice_in_dim(array, begin, begin + length, axis=along)


def flux_divergence(extended, along):
    length = extended.shape[along] - 4
    cell_axis = along - 1
    density = extended[0]
    inverse = 1.0 / density
    normal_vel = extended[along] * inverse
    kinetic = 0.5 * (extended[1] ** 2 + extended[2] ** 2 + extended[3] ** 2) * inverse
    pressure = (gamma_ratio - 1.0) * (extended[4] - kinetic)
    sound = jnp.sqrt(gamma_ratio * pressure * inverse)
    momentum_flux = []
    for component in (1, 2, 3):
        if component == along:
            momentum_flux.append(extended[component] * normal_vel + pressure)
        else:
            momentum_flux.append(extended[component] * normal_vel)
    fluxes = jnp.stack(
        [extended[along]]
        + momentum_flux
        + [(extended[4] + pressure) * normal_vel, extended[5] * normal_vel]
    )
    radius = jnp.abs(normal_vel) + sound
    p_plus = take_range(pressure, 2, length + 2, cell_axis)
    p_here = take_range(pressure, 1, length + 2, cell_axis)
    p_minus = take_range(pressure, 0, length + 2, cell_axis)
    sensor = jnp.abs(p_plus - 2.0 * p_here + p_minus) / (p_plus + 2.0 * p_here + p_minus)
    spread = 0.5 * (
        take_range(radius, 1, length + 1, cell_axis) + take_range(radius, 2, length + 1, cell_axis)
    )
    eps_two = second_coef * jnp.maximum(
        take_range(sensor, 0, length + 1, cell_axis), take_range(sensor, 1, length + 1, cell_axis)
    )
    eps_four = jnp.maximum(0.0, fourth_coef - eps_two)
    first_diff = take_range(extended, 2, length + 1, along) - take_range(
        extended, 1, length + 1, along
    )
    third_diff = (
        take_range(extended, 3, length + 1, along)
        - 3.0 * take_range(extended, 2, length + 1, along)
        + 3.0 * take_range(extended, 1, length + 1, along)
        - take_range(extended, 0, length + 1, along)
    )
    interface = 0.5 * (
        take_range(fluxes, 1, length + 1, along) + take_range(fluxes, 2, length + 1, along)
    ) - spread * (eps_two * first_diff - eps_four * third_diff)
    return take_range(interface, 1, length, along) - take_range(interface, 0, length, along)


def wall_extend(block):
    mirror_sign = jnp.array([1.0, 1.0, -1.0, 1.0, 1.0, 1.0], jnp.float32).reshape(6, 1, 1, 1)
    lower_ghost = block[:, :, 0:2][:, :, ::-1] * mirror_sign
    upper_ghost = block[:, :, -2:][:, :, ::-1] * mirror_sign
    return jnp.concatenate([lower_ghost, block, upper_ghost], axis=2)


def row_residual(block, low_ghost, high_ghost, circum_ext):
    axial_ext = jnp.concatenate([low_ghost, block, high_ghost], axis=1)
    return (
        flux_divergence(axial_ext, 1)
        + flux_divergence(wall_extend(block), 2)
        + flux_divergence(circum_ext, 3)
    )


def local_step(fields, number):
    inverse = 1.0 / fields[:, 0]
    kinetic = 0.5 * (fields[:, 1] ** 2 + fields[:, 2] ** 2 + fields[:, 3] ** 2) * inverse
    pressure = (gamma_ratio - 1.0) * (fields[:, 4] - kinetic)
    sound = jnp.sqrt(gamma_ratio * pressure * inverse)
    speeds = (jnp.abs(fields[:, 1]) + jnp.abs(fields[:, 2]) + jnp.abs(fields[:, 3])) * inverse
    return courant / (speeds + 3.0 * sound + frequency * number / 2.0)


def shifted(payloads, shift):
    count = lax.axis_size("blk")
    pairs = [(source, (source - shift) % count) for source in range(count)]
    rows = [p.reshape(-1, 128) for p in payloads]
    sizes = [r.shape[0] for r in rows]
    moved = lax.ppermute(jnp.concatenate(rows, axis=0) if len(rows) > 1 else rows[0], "blk", pairs)
    pieces, begin = [], 0
    for p, size in zip(payloads, sizes):
        pieces.append(moved[begin:begin + size].reshape(p.shape))
        begin += size
    return pieces


def pick(candidates, index):
    return lax.dynamic_index_in_dim(jnp.stack(candidates), index, 0, keepdims=False)


def signed_digit(value, radix):
    return jnp.mod(value + 1, radix) - 1


def per_device(state, donor_block, donor_offset):
    number = lax.axis_size("inst")
    total_blocks = lax.axis_size("blk")
    own_instance = lax.axis_index("inst")
    own_block = lax.axis_index("blk")
    fields = state[0]
    width = fields.shape[-1]
    faces = jnp.stack([fields[1, :, 0:2], fields[0, :, -2:]])
    faces_below, halo_low = shifted([faces, fields[..., -2:]], -1)
    faces_above, halo_high = shifted([faces, fields[..., :2]], 1)
    near = [faces_below, faces, faces_above]
    padded = jnp.concatenate([halo_low, fields, halo_high], axis=-1)
    windows, mid_digit, top_digit = [], [], []
    for t in range(2):
        rotation = jnp.mod(donor_block[0, t, 0] - own_block, total_blocks)
        low = signed_digit(rotation, 2)
        rest = jnp.mod((rotation - low) // 2, total_blocks // 2)
        mid_digit.append(signed_digit(rest, 4))
        top_digit.append(signed_digit(jnp.mod((rest - mid_digit[t]) // 4, 4), 4))
        offset = donor_offset[0, t, 0] + 0 * rotation
        first = pick([c[t] for c in near], low + 1)
        second = pick([c[t] for c in near], low + 2)
        joined = jnp.concatenate([first, second], axis=-1)
        windows.append(lax.dynamic_slice_in_dim(joined, offset, width, axis=-1))
    windows = jnp.stack(windows)
    mid = [shifted([windows], -2)[0], windows] + [shifted([windows], s)[0] for s in (2, 4)]
    windows = jnp.stack([pick([c[t] for c in mid], mid_digit[t] + 1) for t in range(2)])
    top = [shifted([windows], -8)[0], windows] + [shifted([windows], s)[0] for s in (8, 16)]
    rotor_high, stator_low = [pick([c[t] for c in top], top_digit[t] + 1) for t in range(2)]
    piece = lax.all_gather(state, "inst", axis=0, tiled=True)
    sources = jnp.arange(piece.shape[0], dtype=jnp.int32)
    weights = spectral_weights(own_instance, sources, number)
    spectral = jnp.sum(weights.reshape((-1,) + (1,) * (piece.ndim - 1)) * piece, axis=0)
    rotor = fields[0]
    stator = fields[1]
    rotor_low = jnp.concatenate([rotor[:, 0:1], rotor[:, 0:1]], axis=1)
    stator_high = jnp.concatenate([stator[:, -1:], stator[:, -1:]], axis=1)
    rotor_res = row_residual(rotor, rotor_low, rotor_high, padded[0])
    stator_res = row_residual(stator, stator_low, stator_high, padded[1])
    step = local_step(fields, number)
    residual = jnp.stack([rotor_res, stator_res]) + spectral
    updated = fields - step[:, None] * residual
    return (residual[None], updated[None])


def solution(mesh):
    return jax.shard_map(
        per_device,
        mesh=mesh,
        in_specs=(
            P("inst", None, None, None, None, "blk"),
            P("inst", None, "blk"),
            P("inst", None, "blk"),
        ),
        out_specs=(
            P("inst", None, None, None, None, "blk"),
            P("inst", None, None, None, None, "blk"),
        ),
        check_vma=False,
    )
```

```python
import jax
import jax.numpy as jnp
from jax import lax
from jax.sharding import PartitionSpec as P

gamma_ratio = 1.4
second_coef = 0.5
fourth_coef = 1.0 / 32.0
courant = 0.8
frequency = 0.5


def spectral_weights(target, source, number):
    distance = jnp.mod(target - source, number)
    angle = jnp.pi / number * distance.astype(jnp.float32)
    parity = 1.0 - 2.0 * jnp.mod(distance, 2).astype(jnp.float32)
    nonzero = distance != 0
    sine_safe = jnp.where(nonzero, jnp.sin(angle), 1.0)
    cotangent = jnp.where(nonzero, jnp.cos(angle) / sine_safe, 0.0)
    return parity * (0.25 * frequency + 0.5 * frequency * cotangent)


def take_range(array, begin, length, along):
    return lax.slice_in_dim(array, begin, begin + length, axis=along)


def flux_divergence(extended, along):
    length = extended.shape[along] - 4
    cell_axis = along - 1
    density = extended[0]
    inverse = 1.0 / density
    normal_vel = extended[along] * inverse
    kinetic = 0.5 * (extended[1] ** 2 + extended[2] ** 2 + extended[3] ** 2) * inverse
    pressure = (gamma_ratio - 1.0) * (extended[4] - kinetic)
    sound = jnp.sqrt(gamma_ratio * pressure * inverse)
    momentum_flux = []
    for component in (1, 2, 3):
        if component == along:
            momentum_flux.append(extended[component] * normal_vel + pressure)
        else:
            momentum_flux.append(extended[component] * normal_vel)
    fluxes = jnp.stack(
        [extended[along]]
        + momentum_flux
        + [(extended[4] + pressure) * normal_vel, extended[5] * normal_vel]
    )
    radius = jnp.abs(normal_vel) + sound
    p_plus = take_range(pressure, 2, length + 2, cell_axis)
    p_here = take_range(pressure, 1, length + 2, cell_axis)
    p_minus = take_range(pressure, 0, length + 2, cell_axis)
    sensor = jnp.abs(p_plus - 2.0 * p_here + p_minus) / (p_plus + 2.0 * p_here + p_minus)
    spread = 0.5 * (
        take_range(radius, 1, length + 1, cell_axis) + take_range(radius, 2, length + 1, cell_axis)
    )
    eps_two = second_coef * jnp.maximum(
        take_range(sensor, 0, length + 1, cell_axis), take_range(sensor, 1, length + 1, cell_axis)
    )
    eps_four = jnp.maximum(0.0, fourth_coef - eps_two)
    first_diff = take_range(extended, 2, length + 1, along) - take_range(
        extended, 1, length + 1, along
    )
    third_diff = (
        take_range(extended, 3, length + 1, along)
        - 3.0 * take_range(extended, 2, length + 1, along)
        + 3.0 * take_range(extended, 1, length + 1, along)
        - take_range(extended, 0, length + 1, along)
    )
    interface = 0.5 * (
        take_range(fluxes, 1, length + 1, along) + take_range(fluxes, 2, length + 1, along)
    ) - spread * (eps_two * first_diff - eps_four * third_diff)
    return take_range(interface, 1, length, along) - take_range(interface, 0, length, along)


def wall_extend(block):
    mirror_sign = jnp.array([1.0, 1.0, -1.0, 1.0, 1.0, 1.0], jnp.float32).reshape(6, 1, 1, 1)
    lower_ghost = block[:, :, 0:2][:, :, ::-1] * mirror_sign
    upper_ghost = block[:, :, -2:][:, :, ::-1] * mirror_sign
    return jnp.concatenate([lower_ghost, block, upper_ghost], axis=2)


def row_residual(block, low_ghost, high_ghost, circum_ext):
    axial_ext = jnp.concatenate([low_ghost, block, high_ghost], axis=1)
    return (
        flux_divergence(axial_ext, 1)
        + flux_divergence(wall_extend(block), 2)
        + flux_divergence(circum_ext, 3)
    )


def local_step(fields, number):
    inverse = 1.0 / fields[:, 0]
    kinetic = 0.5 * (fields[:, 1] ** 2 + fields[:, 2] ** 2 + fields[:, 3] ** 2) * inverse
    pressure = (gamma_ratio - 1.0) * (fields[:, 4] - kinetic)
    sound = jnp.sqrt(gamma_ratio * pressure * inverse)
    speeds = (jnp.abs(fields[:, 1]) + jnp.abs(fields[:, 2]) + jnp.abs(fields[:, 3])) * inverse
    return courant / (speeds + 3.0 * sound + frequency * number / 2.0)


def shifted(payloads, shift):
    count = lax.axis_size("blk")
    pairs = [(source, (source - shift) % count) for source in range(count)]
    rows = [p.reshape(-1, 128) for p in payloads]
    sizes = [r.shape[0] for r in rows]
    moved = lax.ppermute(jnp.concatenate(rows, axis=0) if len(rows) > 1 else rows[0], "blk", pairs)
    pieces, begin = [], 0
    for p, size in zip(payloads, sizes):
        pieces.append(moved[begin:begin + size].reshape(p.shape))
        begin += size
    return pieces


def pick(candidates, index):
    return lax.dynamic_index_in_dim(jnp.stack(candidates), index, 0, keepdims=False)


def select_chain(candidates, index):
    chosen = candidates[0]
    for k in range(1, len(candidates)):
        chosen = jnp.where(index == k, candidates[k], chosen)
    return chosen


def signed_digit(value, radix):
    return jnp.mod(value + 1, radix) - 1


def per_device(state, donor_block, donor_offset):
    number = lax.axis_size("inst")
    total_blocks = lax.axis_size("blk")
    own_instance = lax.axis_index("inst")
    own_block = lax.axis_index("blk")
    fields = state[0]
    width = fields.shape[-1]
    faces = jnp.stack([fields[1, :, 0:2], fields[0, :, -2:]])
    faces_below, halo_low = shifted([faces, fields[..., -2:]], -1)
    faces_above, halo_high = shifted([faces, fields[..., :2]], 1)
    near = [faces_below, faces, faces_above]
    padded = jnp.concatenate([halo_low, fields, halo_high], axis=-1)
    windows, mid_digit, top_digit = [], [], []
    for t in range(2):
        rotation = jnp.mod(donor_block[0, t, 0] - own_block, total_blocks)
        low = signed_digit(rotation, 2)
        rest = jnp.mod((rotation - low) // 2, total_blocks // 2)
        mid_digit.append(signed_digit(rest, 4))
        top_digit.append(signed_digit(jnp.mod((rest - mid_digit[t]) // 4, 4), 4))
        first = pick([c[t] for c in near], low + 1)
        second = pick([c[t] for c in near], low + 2)
        joined = jnp.concatenate([first, second], axis=-1)
        windows.append(lax.dynamic_slice_in_dim(joined, donor_offset[0, t, 0], width, axis=-1))
    windows = jnp.stack(windows)
    mid = [shifted([windows], -2)[0], windows] + [shifted([windows], s)[0] for s in (2, 4)]
    windows = jnp.stack([pick([c[t] for c in mid], mid_digit[t] + 1) for t in range(2)])
    top = [shifted([windows], -8)[0], windows] + [shifted([windows], s)[0] for s in (8, 16)]
    rotor_high, stator_low = [select_chain([c[t] for c in top], top_digit[t] + 1) for t in range(2)]
    piece = lax.all_gather(state, "inst", axis=0, tiled=True)
    sources = jnp.arange(piece.shape[0], dtype=jnp.int32)
    weights = spectral_weights(own_instance, sources, number)
    spectral = jnp.sum(weights.reshape((-1,) + (1,) * (piece.ndim - 1)) * piece, axis=0)
    rotor = fields[0]
    stator = fields[1]
    rotor_low = jnp.concatenate([rotor[:, 0:1], rotor[:, 0:1]], axis=1)
    stator_high = jnp.concatenate([stator[:, -1:], stator[:, -1:]], axis=1)
    rotor_res = row_residual(rotor, rotor_low, rotor_high, padded[0])
    stator_res = row_residual(stator, stator_low, stator_high, padded[1])
    step = local_step(fields, number)
    residual = jnp.stack([rotor_res, stator_res]) + spectral
    updated = fields - step[:, None] * residual
    return (residual[None], updated[None])


def solution(mesh):
    return jax.shard_map(
        per_device,
        mesh=mesh,
        in_specs=(
            P("inst", None, None, None, None, "blk"),
            P("inst", None, "blk"),
            P("inst", None, "blk"),
        ),
        out_specs=(
            P("inst", None, None, None, None, "blk"),
            P("inst", None, None, None, None, "blk"),
        ),
        check_vma=False,
    )
```
